256 devices in a mesh: line: 16 (over x, y), plane: 16 (over z, core).
Axes of the slice: x: 4, y: 4, z: 8, core: 2. Of those that a mesh axis runs over, the one named last changes fastest.
Arguments:
- flux_x: float32 [1024, 5, 16384], P('line', None, 'plane'), may hold values from -1600 to 1600
- flux_z: float32 [1024, 5, 16384], P('line', None, 'plane'), may hold values from -1600 to 1600
- viscous: float32 [1024, 16384], P('line', 'plane'), may hold values from 4000 to 16000
- jacobian: float32 [1024, 5, 5, 16384], P('line', None, None, 'plane'), may hold values from -10 to 10
Outputs:
- delta: float32 [1024, 5, 16384], P('line', None, 'plane')
The draws below stay inside these ranges and needn't reach their ends.
All inputs are finite; a program needn't handle non-finite values.
Results may differ from the reference program's by a relative error of at most 0.0003.
Values sent between devices are 32-bit elements; how exact they have to be, the bound alone decides.
No kernel may reach another device: no remote copies, remote signals or barrier semaphores. Data moves between devices by JAX's collectives and lax.ppermute only.
A program may use at most 192 MiB of HBM per device.

```python
import math
import jax
import jax.numpy as jnp
from jax import lax

NVAR = 5
NX = 1024
NZ = 16384


def block_scale(rng, dims, pieces, least, high):
    def one(dim, parts):
        heights = jax.random.uniform(jax.random.fold_in(jax.random.fold_in(rng, 6), dim), (parts,), jnp.float32, least / len(pieces), high / len(pieces))
        return jnp.repeat(jnp.exp(heights), dims[dim] // parts).reshape((-1,) + (1,) * (len(dims) - dim - 1))

    loudness = one(*pieces[0])
    for cut in pieces[1:]:
        loudness = loudness * one(*cut)
    return loudness


def bell_draw(own_key, dims, width, bound, shards=(), kind=jnp.bfloat16):
    level = block_scale(own_key, dims, shards, -0.22, 0.18) if shards else 1.0
    values = jax.random.normal(own_key, dims, jnp.float32) * width * level
    return jnp.minimum(jnp.maximum(values, -bound), bound).astype(kind)


def setup_inputs(seed: int = 0) -> dict:
    key_of = jax.random.split(jax.random.key(seed), 5)
    flux_x = bell_draw(key_of[0], (NX, NVAR, NZ), 200.0, 1600.0, ((0, 16), (2, 16)), jnp.float32)
    flux_z = bell_draw(key_of[1], (NX, NVAR, NZ), 200.0, 1600.0, ((0, 16), (2, 16)), jnp.float32)
    viscous = jnp.clip(jnp.exp(math.log(16000.0) - 1.3862944 * jax.random.uniform(key_of[2], (NX, NZ), jnp.float32) ** block_scale(key_of[2], (NX, NZ), ((0, 16), (1, 16)), -0.2, 0.2)), 4000.0, 16000.0)
    jacobian = jnp.clip(jax.random.uniform(key_of[3], (NX, NVAR, NVAR, NZ), jnp.float32, -10.0, 10.0) * block_scale(key_of[3], (NX, NVAR, NVAR, NZ), ((0, 16), (3, 16)), -0.4, 0.0), -10.0, 10.0)
    return dict(flux_x=flux_x, flux_z=flux_z, viscous=viscous, jacobian=jacobian)


courant = 10.0


def combine_blocks(matrix, operand):
    return jnp.sum(matrix[:, :, None, :] * operand[None, :, :, :], axis=1)


def solve_small(matrix, columns):
    extent = matrix.shape[0]
    for column in range(extent):
        inverse = 1.0 / matrix[column, column]
        pivot_row = matrix[column] * inverse
        column_row = columns[column] * inverse
        factor = matrix[:, column]
        matrix = matrix - factor[:, None, :] * pivot_row[None]
        columns = columns - factor[:, None, :] * column_row[None]
        matrix = matrix.at[column].set(pivot_row)
        columns = columns.at[column].set(column_row)
    return columns


def cell_blocks(viscous, jacobian):
    identity = jnp.eye(5, dtype=jnp.float32)[:, :, None]
    spread = viscous[None, None, :]
    lower_block = -spread * identity - jacobian
    center_block = (1.0 + 2.0 * spread) * identity
    upper_block = -spread * identity + jacobian
    return lower_block, center_block, upper_block


def eliminate(previous, lower_block, center_block, upper_block, source):
    extent = center_block.shape[0]
    schur = center_block - combine_blocks(lower_block, previous[:, :extent])
    moved = source - combine_blocks(lower_block, previous[:, extent:])
    return solve_small(schur, jnp.concatenate([upper_block, moved], 1))


def back_substitute(factors, extent):
    def retreat(following, factor):
        current = factor[:, extent:] - combine_blocks(factor[:, :extent], following)
        return current, current
    initial = jnp.zeros((factors.shape[1], factors.shape[2] - extent, factors.shape[3]), jnp.float32)
    _, values = lax.scan(retreat, initial, factors, reverse=True)
    return values


def reference(flux_x, flux_z, viscous, jacobian):
    pad_x = jnp.pad(flux_x, ((1, 1), (0, 0), (0, 0)))
    pad_z = jnp.pad(flux_z, ((0, 0), (0, 0), (1, 1)))
    source = -0.5 * courant * (pad_x[2:] - pad_x[:-2]) - 0.5 * courant * (pad_z[:, :, 2:] - pad_z[:, :, :-2])
    block_width = math.gcd(NZ, 2048)
    groups = NZ // block_width

    def split_lines(array):
        return jnp.moveaxis(array.reshape(array.shape[:-1] + (groups, block_width)), -2, 0)

    def solve_group(inputs):
        vis_group, jac_group, src_group = inputs

        def advance(previous, cell):
            lower_block, center_block, upper_block = cell_blocks(cell[0], cell[1])
            result = eliminate(previous, lower_block, center_block, upper_block, cell[2][:, None, :])
            return result, result
        initial = jnp.zeros((5, 6, block_width), jnp.float32)
        _, factors = lax.scan(advance, initial, (vis_group, jac_group, src_group))
        return back_substitute(factors, 5)[:, :, 0, :]

    solved = lax.map(solve_group, (split_lines(viscous), split_lines(jacobian), split_lines(source)))
    return jnp.moveaxis(solved, 0, -2).reshape(NX, 5, NZ)
```

```python
import jax
import jax.numpy as jnp
from jax import lax
from jax.experimental import pallas as pl
from jax.experimental.pallas import tpu as pltpu
from jax.sharding import PartitionSpec as P

courant = 10.0
NV = 5


def padded(block, sides, width):
    for axis, dim in sides:
        count = lax.axis_size(axis)
        forward = [(i, i + 1) for i in range(count - 1)]
        backward = [(target, source) for source, target in forward]
        low = lax.ppermute(
            lax.slice_in_dim(block, block.shape[dim] - width, None, axis=dim), axis, forward
        )
        high = lax.ppermute(lax.slice_in_dim(block, 0, width, axis=dim), axis, backward)
        block = jnp.concatenate([low, block, high], axis=dim)
    return block


def matmul(a, b, rows, inner, cols):
    out = []
    for r in range(rows):
        line = []
        for c in range(cols):
            acc = a[r][0] * b[0][c]
            for k in range(1, inner):
                acc = acc + a[r][k] * b[k][c]
            line.append(acc)
        out.append(line)
    return out


def gauss_jordan(matrix, columns):
    matrix = [row[:] for row in matrix]
    columns = [row[:] for row in columns]
    for k in range(NV):
        inverse = 1.0 / matrix[k][k]
        pivot = [matrix[k][j] * inverse for j in range(k + 1, NV)]
        chosen = [x * inverse for x in columns[k]]
        for r in range(NV):
            if r == k:
                continue
            factor = matrix[r][k]
            for jj, j in enumerate(range(k + 1, NV)):
                matrix[r][j] = matrix[r][j] - factor * pivot[jj]
            columns[r] = [x - factor * y for x, y in zip(columns[r], chosen)]
        matrix[k] = [None] * (k + 1) + pivot
        columns[k] = chosen
    return columns


def grid_of(flat, rows, cols):
    return [[flat[r * cols + c] for c in range(cols)] for r in range(rows)]


def flat_of(grid):
    return [x for row in grid for x in row]


def factor_kernel(vis_ref, jac_ref, src_ref, out_ref):
    cells = vis_ref.shape[0]
    tile = vis_ref.shape[1:]
    zero = jnp.zeros(tile, jnp.float32)
    one = jnp.ones(tile, jnp.float32)

    def forward(i, carry):
        c_prev = grid_of(carry[0:25], NV, NV)
        g_prev = [[x] for x in carry[25:30]]
        w_prev = grid_of(carry[30:55], NV, NV)
        spread = vis_ref[i]
        jac = [[jac_ref[i, a * NV + b] for b in range(NV)] for a in range(NV)]
        lower = [[(-spread - jac[a][b]) if a == b else (-jac[a][b]) for b in range(NV)] for a in range(NV)]
        upper = [[(-spread + jac[a][b]) if a == b else jac[a][b] for b in range(NV)] for a in range(NV)]
        centre = 1.0 + 2.0 * spread
        lc = matmul(lower, c_prev, NV, NV, NV)
        schur = [[(centre - lc[a][c]) if a == c else (-lc[a][c]) for c in range(NV)] for a in range(NV)]
        lg = matmul(lower, g_prev, NV, NV, 1)
        lw = matmul(lower, w_prev, NV, NV, NV)
        cols = []
        for a in range(NV):
            cols.append(upper[a] + [src_ref[i, a] - lg[a][0]] + [-x for x in lw[a]])
        sol = gauss_jordan(schur, cols)
        c_new = [row[0:NV] for row in sol]
        g_new = [row[NV] for row in sol]
        w_new = [row[NV + 1:] for row in sol]
        flat = flat_of(c_new) + g_new + flat_of(w_new)
        for k in range(55):
            out_ref[i, k] = flat[k]
        return tuple(flat)

    init = [zero] * 30 + flat_of([[(-one if a == b else zero) for b in range(NV)] for a in range(NV)])
    lax.fori_loop(0, cells, forward, tuple(init))

    def backward(step, carry):
        i = cells - 1 - step
        nxt = [[carry[a]] + list(carry[5 + a * 5:10 + a * 5]) + list(carry[30 + a * 5:35 + a * 5]) for a in range(NV)]
        c_i = [[out_ref[i, a * NV + b] for b in range(NV)] for a in range(NV)]
        g_i = [out_ref[i, 25 + a] for a in range(NV)]
        w_i = [[out_ref[i, 30 + a * NV + b] for b in range(NV)] for a in range(NV)]
        prod = matmul(c_i, nxt, NV, NV, 11)
        y = [g_i[a] - prod[a][0] for a in range(NV)]
        w = [[w_i[a][b] - prod[a][1 + b] for b in range(NV)] for a in range(NV)]
        v = [[-prod[a][6 + b] for b in range(NV)] for a in range(NV)]
        flat = y + flat_of(w) + flat_of(v)
        for k in range(55):
            out_ref[i, k] = flat[k]
        return tuple(flat)

    init = [zero] * 30 + flat_of([[(-one if a == b else zero) for b in range(NV)] for a in range(NV)])
    lax.fori_loop(0, cells, backward, tuple(init))


def reduced_kernel(tail_ref, head_ref, out_ref, keep_ref):
    steps = tail_ref.shape[0]
    lanes = tail_ref.shape[2]

    def row(ref, q, k):
        return ref[q, k:k + 1, :]

    def forward(q, carry):
        x_prev = grid_of(carry[0:25], NV, NV)
        u_prev = [[x] for x in carry[25:30]]
        y63 = [row(tail_ref, q, a) for a in range(NV)]
        w63 = [[row(tail_ref, q, 5 + a * NV + b) for b in range(NV)] for a in range(NV)]
        v63 = [[row(tail_ref, q, 30 + a * NV + b) for b in range(NV)] for a in range(NV)]
        y0 = [row(head_ref, q, a) for a in range(NV)]
        w0 = [[row(head_ref, q, 5 + a * NV + b) for b in range(NV)] for a in range(NV)]
        v0 = [[row(head_ref, q, 30 + a * NV + b) for b in range(NV)] for a in range(NV)]
        wx = matmul(w63, x_prev, NV, NV, NV)
        m = [[v63[a][b] - wx[a][b] for b in range(NV)] for a in range(NV)]
        wu = matmul(w63, u_prev, NV, NV, 1)
        av = [[y63[a] - wu[a][0]] for a in range(NV)]
        wm = matmul(w0, m, NV, NV, NV)
        k_mat = [[(1.0 - wm[a][b]) if a == b else (-wm[a][b]) for b in range(NV)] for a in range(NV)]
        wa = matmul(w0, av, NV, NV, 1)
        cols = [v0[a] + [y0[a] - wa[a][0]] for a in range(NV)]
        sol = gauss_jordan(k_mat, cols)
        y_new = [r[0:NV] for r in sol]
        v_new = [[r[NV]] for r in sol]
        my = matmul(m, y_new, NV, NV, NV)
        x_new = [[-my[a][b] for b in range(NV)] for a in range(NV)]
        mv = matmul(m, v_new, NV, NV, 1)
        u_new = [av[a][0] - mv[a][0] for a in range(NV)]
        flat = flat_of(x_new) + flat_of(y_new) + u_new + [r[0] for r in v_new]
        for k in range(60):
            keep_ref[q, k:k + 1, :] = flat[k]
        return tuple(flat[0:25] + u_new)

    zero = jnp.zeros((1, lanes), jnp.float32)
    lax.fori_loop(0, steps, forward, tuple([zero] * 30))

    h_next = [[zero] for _ in range(NV)]
    for q in range(steps - 1, -1, -1):
        x_q = [[keep_ref[q, a * NV + b:a * NV + b + 1, :] for b in range(NV)] for a in range(NV)]
        y_q = [[keep_ref[q, 25 + a * NV + b:26 + a * NV + b, :] for b in range(NV)] for a in range(NV)]
        u_q = [keep_ref[q, 50 + a:51 + a, :] for a in range(NV)]
        v_q = [keep_ref[q, 55 + a:56 + a, :] for a in range(NV)]
        xh = matmul(x_q, h_next, NV, NV, 1)
        yh = matmul(y_q, h_next, NV, NV, 1)
        t_prev = [u_q[a] - xh[a][0] for a in range(NV)]
        h_here = [v_q[a] - yh[a][0] for a in range(NV)]
        if q <= steps - 2:
            for a in range(NV):
                out_ref[q, a:a + 1, :] = t_prev[a]
        if q >= 1:
            for a in range(NV):
                out_ref[q - 1, 5 + a:6 + a, :] = h_here[a]
        h_next = [[x] for x in h_here]


def whole(shape):
    return jax.ShapeDtypeStruct(shape, jnp.float32)


def per_device(flux_x, flux_z, viscous, jacobian):
    cells, line_count = viscous.shape
    rows = line_count // 128
    parts = lax.axis_size("line")
    stream = padded(flux_x, (("line", 0),), 1)
    across = padded(flux_z, (("plane", 2),), 1)
    source = -0.5 * courant * (stream[2:] - stream[:-2]) - 0.5 * courant * (
        across[:, :, 2:] - across[:, :, :-2]
    )
    src4 = source.reshape(cells, NV, rows, 128)
    jac4 = jacobian.reshape(cells, NV * NV, rows, 128)
    vis3 = viscous.reshape(cells, rows, 128)
    vmem = pl.BlockSpec(memory_space=pltpu.VMEM)
    factors = pl.pallas_call(
        factor_kernel,
        out_shape=whole((cells, 55, rows, 128)),
        in_specs=[vmem, vmem, vmem],
        out_specs=vmem,
        compiler_params=pltpu.CompilerParams(vmem_limit_bytes=60 * 1024 * 1024),
    )(vis3, jac4, src4)

    ends = jnp.stack([factors[0], factors[cells - 1]]).reshape(2 * 55, line_count)
    chunk = line_count // parts
    gathered = lax.all_to_all(ends, "line", 1, 0, tiled=True).reshape(parts, 2, 55, chunk)
    empty = jnp.zeros((1, 55, chunk), jnp.float32)
    tails = jnp.concatenate([empty, gathered[:, 1]], 0)
    heads = jnp.concatenate([gathered[:, 0], empty], 0)
    answers = pl.pallas_call(
        reduced_kernel,
        out_shape=whole((parts, 10, chunk)),
        in_specs=[vmem, vmem],
        out_specs=vmem,
        scratch_shapes=[pltpu.VMEM((parts + 1, 60, chunk), jnp.float32)],
    )(tails, heads)
    back = lax.all_to_all(answers, "line", 0, 0, tiled=True)
    bounds = jnp.moveaxis(back, 0, 1).reshape(10, rows, 128)
    before = bounds[0:NV]
    after = bounds[NV:]
    local = factors[:, 0:NV]
    w = factors[:, 5:30].reshape(cells, NV, NV, rows, 128)
    v = factors[:, 30:55].reshape(cells, NV, NV, rows, 128)
    delta = local - jnp.sum(w * before[None, None], axis=2) - jnp.sum(v * after[None, None], axis=2)
    return delta.reshape(cells, NV, line_count)


def solution(mesh):
    placed = (
        P("line", None, "plane"),
        P("line", None, "plane"),
        P("line", "plane"),
        P("line", None, None, "plane"),
    )
    return jax.shard_map(
        per_device, mesh=mesh, in_specs=placed, out_specs=P("line", None, "plane"), check_vma=False
    )
```

```python
import jax
import jax.numpy as jnp
from jax import lax
from jax.experimental import pallas as pl
from jax.experimental.pallas import tpu as pltpu
from jax.sharding import PartitionSpec as P

courant = 10.0
NV = 5


def padded(block, sides, width):
    for axis, dim in sides:
        count = lax.axis_size(axis)
        forward = [(i, i + 1) for i in range(count - 1)]
        backward = [(target, source) for source, target in forward]
        low = lax.ppermute(
            lax.slice_in_dim(block, block.shape[dim] - width, None, axis=dim), axis, forward
        )
        high = lax.ppermute(lax.slice_in_dim(block, 0, width, axis=dim), axis, backward)
        block = jnp.concatenate([low, block, high], axis=dim)
    return block


def matmul(a, b, rows, inner, cols):
    out = []
    for r in range(rows):
        line = []
        for c in range(cols):
            acc = a[r][0] * b[0][c]
            for k in range(1, inner):
                acc = acc + a[r][k] * b[k][c]
            line.append(acc)
        out.append(line)
    return out


def gauss_jordan(matrix, columns):
    matrix = [row[:] for row in matrix]
    columns = [row[:] for row in columns]
    for k in range(NV):
        inverse = 1.0 / matrix[k][k]
        pivot = [matrix[k][j] * inverse for j in range(k + 1, NV)]
        chosen = [x * inverse for x in columns[k]]
        for r in range(NV):
            if r == k:
                continue
            factor = matrix[r][k]
            for jj, j in enumerate(range(k + 1, NV)):
                matrix[r][j] = matrix[r][j] - factor * pivot[jj]
            columns[r] = [x - factor * y for x, y in zip(columns[r], chosen)]
        matrix[k] = [None] * (k + 1) + pivot
        columns[k] = chosen
    return columns


def grid_of(flat, rows, cols):
    return [[flat[r * cols + c] for c in range(cols)] for r in range(rows)]


def flat_of(grid):
    return [x for row in grid for x in row]


def factor_kernel(vis_ref, jac_ref, src_ref, out_ref):
    cells = out_ref.shape[0]
    tile = out_ref.shape[2:]
    rows = tile[0]
    zero = jnp.zeros(tile, jnp.float32)
    one = jnp.ones(tile, jnp.float32)

    def forward(i, carry):
        c_prev = grid_of(carry[0:25], NV, NV)
        g_prev = [[x] for x in carry[25:30]]
        w_prev = grid_of(carry[30:55], NV, NV)
        block = i // 8
        picked = pl.ds(i % 8, rows, stride=8)
        spread = vis_ref[block, picked, :]
        jac = [[jac_ref[a * NV + b, block, picked, :] for b in range(NV)] for a in range(NV)]
        lower = [[(-spread - jac[a][b]) if a == b else (-jac[a][b]) for b in range(NV)] for a in range(NV)]
        upper = [[(-spread + jac[a][b]) if a == b else jac[a][b] for b in range(NV)] for a in range(NV)]
        centre = 1.0 + 2.0 * spread
        lc = matmul(lower, c_prev, NV, NV, NV)
        schur = [[(centre - lc[a][c]) if a == c else (-lc[a][c]) for c in range(NV)] for a in range(NV)]
        lg = matmul(lower, g_prev, NV, NV, 1)
        lw = matmul(lower, w_prev, NV, NV, NV)
        cols = []
        for a in range(NV):
            cols.append(upper[a] + [src_ref[a, block, picked, :] - lg[a][0]] + [-x for x in lw[a]])
        sol = gauss_jordan(schur, cols)
        c_new = [row[0:NV] for row in sol]
        g_new = [row[NV] for row in sol]
        w_new = [row[NV + 1:] for row in sol]
        flat = flat_of(c_new) + g_new + flat_of(w_new)
        for k in range(55):
            out_ref[i, k] = flat[k]
        return tuple(flat)

    init = [zero] * 30 + flat_of([[(-one if a == b else zero) for b in range(NV)] for a in range(NV)])
    lax.fori_loop(0, cells, forward, tuple(init))

    def backward(step, carry):
        i = cells - 1 - step
        nxt = [[carry[a]] + list(carry[5 + a * 5:10 + a * 5]) + list(carry[30 + a * 5:35 + a * 5]) for a in range(NV)]
        c_i = [[out_ref[i, a * NV + b] for b in range(NV)] for a in range(NV)]
        g_i = [out_ref[i, 25 + a] for a in range(NV)]
        w_i = [[out_ref[i, 30 + a * NV + b] for b in range(NV)] for a in range(NV)]
        prod = matmul(c_i, nxt, NV, NV, 11)
        y = [g_i[a] - prod[a][0] for a in range(NV)]
        w = [[w_i[a][b] - prod[a][1 + b] for b in range(NV)] for a in range(NV)]
        v = [[-prod[a][6 + b] for b in range(NV)] for a in range(NV)]
        flat = y + flat_of(w) + flat_of(v)
        for k in range(55):
            out_ref[i, k] = flat[k]
        return tuple(flat)

    init = [zero] * 30 + flat_of([[(-one if a == b else zero) for b in range(NV)] for a in range(NV)])
    lax.fori_loop(0, cells, backward, tuple(init))


def interface_step(tail, head, carry):
    x_prev = grid_of(carry[0:25], NV, NV)
    u_prev = [[x] for x in carry[25:30]]
    y63 = tail[0:5]
    w63 = grid_of(tail[5:30], NV, NV)
    v63 = grid_of(tail[30:55], NV, NV)
    y0 = head[0:5]
    w0 = grid_of(head[5:30], NV, NV)
    v0 = grid_of(head[30:55], NV, NV)
    wx = matmul(w63, x_prev, NV, NV, NV)
    m = [[v63[a][b] - wx[a][b] for b in range(NV)] for a in range(NV)]
    wu = matmul(w63, u_prev, NV, NV, 1)
    av = [[y63[a] - wu[a][0]] for a in range(NV)]
    wm = matmul(w0, m, NV, NV, NV)
    k_mat = [[(1.0 - wm[a][b]) if a == b else (-wm[a][b]) for b in range(NV)] for a in range(NV)]
    wa = matmul(w0, av, NV, NV, 1)
    cols = [v0[a] + [y0[a] - wa[a][0]] for a in range(NV)]
    sol = gauss_jordan(k_mat, cols)
    y_new = [r[0:NV] for r in sol]
    v_new = [[r[NV]] for r in sol]
    my = matmul(m, y_new, NV, NV, NV)
    x_new = [[-my[a][b] for b in range(NV)] for a in range(NV)]
    mv = matmul(m, v_new, NV, NV, 1)
    u_new = [av[a][0] - mv[a][0] for a in range(NV)]
    flat = flat_of(x_new) + flat_of(y_new) + u_new + [r[0] for r in v_new]
    return flat, tuple(flat[0:25] + u_new)


def reduced_kernel(ends_ref, out_ref, keep_ref):
    parts = ends_ref.shape[0]
    lanes = ends_ref.shape[2]
    zero = jnp.zeros((1, lanes), jnp.float32)

    def rows_of(p, first):
        return [ends_ref[p, first + k:first + k + 1, :] for k in range(55)]

    def keep(q, flat):
        for k in range(60):
            keep_ref[q, k:k + 1, :] = flat[k]

    flat, carry = interface_step([zero] * 55, rows_of(0, 0), tuple([zero] * 30))
    keep(0, flat)

    def forward(q, carry):
        flat, carry = interface_step(rows_of(q - 1, 55), rows_of(q, 0), carry)
        keep(q, flat)
        return carry

    carry = lax.fori_loop(1, parts, forward, carry)
    flat, carry = interface_step(rows_of(parts - 1, 55), [zero] * 55, carry)
    keep(parts, flat)

    h_next = [[zero] for _ in range(NV)]
    for q in range(parts, -1, -1):
        x_q = [[keep_ref[q, a * NV + b:a * NV + b + 1, :] for b in range(NV)] for a in range(NV)]
        y_q = [[keep_ref[q, 25 + a * NV + b:26 + a * NV + b, :] for b in range(NV)] for a in range(NV)]
        u_q = [keep_ref[q, 50 + a:51 + a, :] for a in range(NV)]
        v_q = [keep_ref[q, 55 + a:56 + a, :] for a in range(NV)]
        xh = matmul(x_q, h_next, NV, NV, 1)
        yh = matmul(y_q, h_next, NV, NV, 1)
        t_prev = [u_q[a] - xh[a][0] for a in range(NV)]
        h_here = [v_q[a] - yh[a][0] for a in range(NV)]
        if q <= parts - 1:
            for a in range(NV):
                out_ref[q, a:a + 1, :] = t_prev[a]
        if q >= 1:
            for a in range(NV):
                out_ref[q - 1, 5 + a:6 + a, :] = h_here[a]
        h_next = [[x] for x in h_here]


def combine_kernel(fac_ref, bnd_ref, out_ref):
    rows = fac_ref.shape[2]
    before = [bnd_ref[b] for b in range(NV)]
    after = [bnd_ref[NV + b] for b in range(NV)]
    for c in range(fac_ref.shape[0]):
        for a in range(NV):
            w_t = fac_ref[c, 5 + a * NV] * before[0]
            v_h = fac_ref[c, 30 + a * NV] * after[0]
            for b in range(1, NV):
                w_t = w_t + fac_ref[c, 5 + a * NV + b] * before[b]
                v_h = v_h + fac_ref[c, 30 + a * NV + b] * after[b]
            out_ref[a, 0, pl.ds(c, rows, stride=8), :] = fac_ref[c, a] - w_t - v_h


def whole(shape):
    return jax.ShapeDtypeStruct(shape, jnp.float32)


def stored_order(array, lead):
    *head, cells, lines = array.shape
    rows = lines // 128
    split = array.reshape(*head, cells // 8, 8, rows, 128)
    return jnp.swapaxes(split, -3, -2).reshape(*head, cells // 8, rows * 8, 128)


def per_device(flux_x, flux_z, viscous, jacobian):
    cells, line_count = viscous.shape
    rows = line_count // 128
    parts = lax.axis_size("line")
    chunk = line_count // parts
    stream = padded(flux_x, (("line", 0),), 1)
    across = padded(flux_z, (("plane", 2),), 1)
    source = -0.5 * courant * (stream[2:] - stream[:-2]) - 0.5 * courant * (
        across[:, :, 2:] - across[:, :, :-2]
    )
    src_s = stored_order(jnp.transpose(source, (1, 0, 2)), 1)
    jac_s = stored_order(jnp.transpose(jacobian, (1, 2, 0, 3)).reshape(NV * NV, cells, line_count), 1)
    vis_s = stored_order(viscous, 0)
    vmem = pl.BlockSpec(memory_space=pltpu.VMEM)
    factors = pl.pallas_call(
        factor_kernel,
        out_shape=whole((cells, 55, rows, 128)),
        in_specs=[vmem, vmem, vmem],
        out_specs=vmem,
        compiler_params=pltpu.CompilerParams(vmem_limit_bytes=60 * 1024 * 1024),
    )(vis_s, jac_s, src_s)

    ends = jnp.stack([factors[0], factors[cells - 1]]).reshape(2 * 55, parts, chunk)
    sent = jnp.transpose(ends, (1, 0, 2))
    gathered = lax.all_to_all(sent, "line", 0, 0, tiled=True)
    answers = pl.pallas_call(
        reduced_kernel,
        out_shape=whole((parts, 10, chunk)),
        in_specs=[vmem],
        out_specs=vmem,
        scratch_shapes=[pltpu.VMEM((parts + 1, 60, chunk), jnp.float32)],
    )(gathered)
    back = lax.all_to_all(answers, "line", 0, 0, tiled=True)
    bounds = jnp.moveaxis(back, 1, 0).reshape(10, rows, 128)
    blocks = cells // 8
    delta_s = pl.pallas_call(
        combine_kernel,
        out_shape=whole((NV, blocks, rows * 8, 128)),
        grid=(blocks,),
        in_specs=[
            pl.BlockSpec((8, 55, rows, 128), lambda c: (c, 0, 0, 0)),
            pl.BlockSpec((10, rows, 128), lambda c: (0, 0, 0)),
        ],
        out_specs=pl.BlockSpec((NV, 1, rows * 8, 128), lambda c: (0, c, 0, 0)),
    )(factors, bounds)
    delta = jnp.swapaxes(delta_s.reshape(NV, blocks, rows, 8, 128), 2, 3).reshape(NV, cells, line_count)
    return jnp.transpose(delta, (1, 0, 2))


def solution(mesh):
    placed = (
        P("line", None, "plane"),
        P("line", None, "plane"),
        P("line", "plane"),
        P("line", None, None, "plane"),
    )
    return jax.shard_map(
        per_device, mesh=mesh, in_specs=placed, out_specs=P("line", None, "plane"), check_vma=False
    )
```

```python
import jax
import jax.numpy as jnp
from jax import lax
from jax.experimental import pallas as pl
from jax.experimental.pallas import tpu as pltpu
from jax.sharding import PartitionSpec as P

courant = 10.0
NV = 5


def padded(block, sides, width):
    for axis, dim in sides:
        count = lax.axis_size(axis)
        forward = [(i, i + 1) for i in range(count - 1)]
        backward = [(target, source) for source, target in forward]
        low = lax.ppermute(
            lax.slice_in_dim(block, block.shape[dim] - width, None, axis=dim), axis, forward
        )
        high = lax.ppermute(lax.slice_in_dim(block, 0, width, axis=dim), axis, backward)
        block = jnp.concatenate([low, block, high], axis=dim)
    return block


def matmul(a, b, rows, inner, cols):
    out = []
    for r in range(rows):
        line = []
        for c in range(cols):
            acc = a[r][0] * b[0][c]
            for k in range(1, inner):
                acc = acc + a[r][k] * b[k][c]
            line.append(acc)
        out.append(line)
    return out


def gauss_jordan(matrix, columns):
    matrix = [row[:] for row in matrix]
    columns = [row[:] for row in columns]
    for k in range(NV):
        inverse = 1.0 / matrix[k][k]
        pivot = [matrix[k][j] * inverse for j in range(k + 1, NV)]
        chosen = [x * inverse for x in columns[k]]
        for r in range(NV):
            if r == k:
                continue
            factor = matrix[r][k]
            for jj, j in enumerate(range(k + 1, NV)):
                matrix[r][j] = matrix[r][j] - factor * pivot[jj]
            columns[r] = [x - factor * y for x, y in zip(columns[r], chosen)]
        matrix[k] = [None] * (k + 1) + pivot
        columns[k] = chosen
    return columns


def grid_of(flat, rows, cols):
    return [[flat[r * cols + c] for c in range(cols)] for r in range(rows)]


def flat_of(grid):
    return [x for row in grid for x in row]


def factor_kernel(vis_hbm, jac_hbm, src_hbm, out_hbm, vis_ref, jac_ref, src_ref, out_ref, in_sem, out_sem):
    cells = out_ref.shape[0]
    blocks = cells // 8
    tile = out_ref.shape[2:]
    rows = tile[0]
    zero = jnp.zeros(tile, jnp.float32)
    one = jnp.ones(tile, jnp.float32)

    def arrivals(b):
        return [
            pltpu.make_async_copy(vis_hbm.at[b], vis_ref.at[b], in_sem.at[0, b]),
            pltpu.make_async_copy(jac_hbm.at[:, b], jac_ref.at[:, b], in_sem.at[1, b]),
            pltpu.make_async_copy(src_hbm.at[:, b], src_ref.at[:, b], in_sem.at[2, b]),
        ]

    def departure(b):
        return pltpu.make_async_copy(out_ref.at[pl.ds(b * 8, 8)], out_hbm.at[pl.ds(b * 8, 8)], out_sem.at[b])

    for b in range(blocks):
        for copy in arrivals(b):
            copy.start()

    def forward(i, carry):
        @pl.when(i % 8 == 0)
        def _():
            for copy in arrivals(i // 8):
                copy.wait()

        c_prev = grid_of(carry[0:25], NV, NV)
        g_prev = [[x] for x in carry[25:30]]
        w_prev = grid_of(carry[30:55], NV, NV)
        block = i // 8
        picked = pl.ds(i % 8, rows, stride=8)
        spread = vis_ref[block, picked, :]
        jac = [[jac_ref[a * NV + b, block, picked, :] for b in range(NV)] for a in range(NV)]
        lower = [[(-spread - jac[a][b]) if a == b else (-jac[a][b]) for b in range(NV)] for a in range(NV)]
        upper = [[(-spread + jac[a][b]) if a == b else jac[a][b] for b in range(NV)] for a in range(NV)]
        centre = 1.0 + 2.0 * spread
        lc = matmul(lower, c_prev, NV, NV, NV)
        schur = [[(centre - lc[a][c]) if a == c else (-lc[a][c]) for c in range(NV)] for a in range(NV)]
        lg = matmul(lower, g_prev, NV, NV, 1)
        lw = matmul(lower, w_prev, NV, NV, NV)
        cols = []
        for a in range(NV):
            cols.append(upper[a] + [src_ref[a, block, picked, :] - lg[a][0]] + [-x for x in lw[a]])
        sol = gauss_jordan(schur, cols)
        c_new = [row[0:NV] for row in sol]
        g_new = [row[NV] for row in sol]
        w_new = [row[NV + 1:] for row in sol]
        flat = flat_of(c_new) + g_new + flat_of(w_new)
        for k in range(55):
            out_ref[i, k] = flat[k]
        return tuple(flat)

    init = [zero] * 30 + flat_of([[(-one if a == b else zero) for b in range(NV)] for a in range(NV)])
    lax.fori_loop(0, cells, forward, tuple(init))

    def backward(step, carry):
        i = cells - 1 - step
        nxt = [[carry[a]] + list(carry[5 + a * 5:10 + a * 5]) + list(carry[30 + a * 5:35 + a * 5]) for a in range(NV)]
        c_i = [[out_ref[i, a * NV + b] for b in range(NV)] for a in range(NV)]
        g_i = [out_ref[i, 25 + a] for a in range(NV)]
        w_i = [[out_ref[i, 30 + a * NV + b] for b in range(NV)] for a in range(NV)]
        prod = matmul(c_i, nxt, NV, NV, 11)
        y = [g_i[a] - prod[a][0] for a in range(NV)]
        w = [[w_i[a][b] - prod[a][1 + b] for b in range(NV)] for a in range(NV)]
        v = [[-prod[a][6 + b] for b in range(NV)] for a in range(NV)]
        flat = y + flat_of(w) + flat_of(v)
        for k in range(55):
            out_ref[i, k] = flat[k]

        @pl.when(i % 8 == 0)
        def _():
            departure(i // 8).start()

        return tuple(flat)

    init = [zero] * 30 + flat_of([[(-one if a == b else zero) for b in range(NV)] for a in range(NV)])
    lax.fori_loop(0, cells, backward, tuple(init))
    for b in range(blocks):
        departure(b).wait()


def interface_step(tail, head, carry):
    x_prev = grid_of(carry[0:25], NV, NV)
    u_prev = [[x] for x in carry[25:30]]
    y63 = tail[0:5]
    w63 = grid_of(tail[5:30], NV, NV)
    v63 = grid_of(tail[30:55], NV, NV)
    y0 = head[0:5]
    w0 = grid_of(head[5:30], NV, NV)
    v0 = grid_of(head[30:55], NV, NV)
    wx = matmul(w63, x_prev, NV, NV, NV)
    m = [[v63[a][b] - wx[a][b] for b in range(NV)] for a in range(NV)]
    wu = matmul(w63, u_prev, NV, NV, 1)
    av = [[y63[a] - wu[a][0]] for a in range(NV)]
    wm = matmul(w0, m, NV, NV, NV)
    k_mat = [[(1.0 - wm[a][b]) if a == b else (-wm[a][b]) for b in range(NV)] for a in range(NV)]
    wa = matmul(w0, av, NV, NV, 1)
    cols = [v0[a] + [y0[a] - wa[a][0]] for a in range(NV)]
    sol = gauss_jordan(k_mat, cols)
    y_new = [r[0:NV] for r in sol]
    v_new = [[r[NV]] for r in sol]
    my = matmul(m, y_new, NV, NV, NV)
    x_new = [[-my[a][b] for b in range(NV)] for a in range(NV)]
    mv = matmul(m, v_new, NV, NV, 1)
    u_new = [av[a][0] - mv[a][0] for a in range(NV)]
    flat = flat_of(x_new) + flat_of(y_new) + u_new + [r[0] for r in v_new]
    return flat, tuple(flat[0:25] + u_new)


def reduced_kernel(ends_ref, out_ref, keep_ref):
    parts = ends_ref.shape[0]
    lanes = ends_ref.shape[2]
    zero = jnp.zeros((1, lanes), jnp.float32)

    def rows_of(p, first):
        return [ends_ref[p, first + k:first + k + 1, :] for k in range(55)]

    def keep(q, flat):
        for k in range(60):
            keep_ref[q, k:k + 1, :] = flat[k]

    flat, carry = interface_step([zero] * 55, rows_of(0, 0), tuple([zero] * 30))
    keep(0, flat)

    def forward(q, carry):
        flat, carry = interface_step(rows_of(q - 1, 55), rows_of(q, 0), carry)
        keep(q, flat)
        return carry

    carry = lax.fori_loop(1, parts, forward, carry)
    flat, carry = interface_step(rows_of(parts - 1, 55), [zero] * 55, carry)
    keep(parts, flat)

    h_next = [[zero] for _ in range(NV)]
    for q in range(parts, -1, -1):
        x_q = [[keep_ref[q, a * NV + b:a * NV + b + 1, :] for b in range(NV)] for a in range(NV)]
        y_q = [[keep_ref[q, 25 + a * NV + b:26 + a * NV + b, :] for b in range(NV)] for a in range(NV)]
        u_q = [keep_ref[q, 50 + a:51 + a, :] for a in range(NV)]
        v_q = [keep_ref[q, 55 + a:56 + a, :] for a in range(NV)]
        xh = matmul(x_q, h_next, NV, NV, 1)
        yh = matmul(y_q, h_next, NV, NV, 1)
        t_prev = [u_q[a] - xh[a][0] for a in range(NV)]
        h_here = [v_q[a] - yh[a][0] for a in range(NV)]
        if q <= parts - 1:
            for a in range(NV):
                out_ref[q, a:a + 1, :] = t_prev[a]
        if q >= 1:
            for a in range(NV):
                out_ref[q - 1, 5 + a:6 + a, :] = h_here[a]
        h_next = [[x] for x in h_here]


def combine_kernel(fac_ref, bnd_ref, out_ref):
    rows = fac_ref.shape[2]
    before = [bnd_ref[b] for b in range(NV)]
    after = [bnd_ref[NV + b] for b in range(NV)]
    for c in range(fac_ref.shape[0]):
        for a in range(NV):
            w_t = fac_ref[c, 5 + a * NV] * before[0]
            v_h = fac_ref[c, 30 + a * NV] * after[0]
            for b in range(1, NV):
                w_t = w_t + fac_ref[c, 5 + a * NV + b] * before[b]
                v_h = v_h + fac_ref[c, 30 + a * NV + b] * after[b]
            out_ref[a, 0, pl.ds(c, rows, stride=8), :] = fac_ref[c, a] - w_t - v_h


def whole(shape):
    return jax.ShapeDtypeStruct(shape, jnp.float32)


def stored_order(array, lead):
    *head, cells, lines = array.shape
    rows = lines // 128
    split = array.reshape(*head, cells // 8, 8, rows, 128)
    return jnp.swapaxes(split, -3, -2).reshape(*head, cells // 8, rows * 8, 128)


def per_device(flux_x, flux_z, viscous, jacobian):
    cells, line_count = viscous.shape
    rows = line_count // 128
    parts = lax.axis_size("line")
    chunk = line_count // parts
    stream = padded(flux_x, (("line", 0),), 1)
    across = padded(flux_z, (("plane", 2),), 1)
    source = -0.5 * courant * (stream[2:] - stream[:-2]) - 0.5 * courant * (
        across[:, :, 2:] - across[:, :, :-2]
    )
    src_s = stored_order(jnp.transpose(source, (1, 0, 2)), 1)
    jac_s = stored_order(jnp.transpose(jacobian, (1, 2, 0, 3)).reshape(NV * NV, cells, line_count), 1)
    vis_s = stored_order(viscous, 0)
    vmem = pl.BlockSpec(memory_space=pltpu.VMEM)
    hbm = pl.BlockSpec(memory_space=pl.ANY)
    factors = pl.pallas_call(
        factor_kernel,
        out_shape=whole((cells, 55, rows, 128)),
        in_specs=[hbm, hbm, hbm],
        out_specs=hbm,
        scratch_shapes=[
            pltpu.VMEM(vis_s.shape, jnp.float32),
            pltpu.VMEM(jac_s.shape, jnp.float32),
            pltpu.VMEM(src_s.shape, jnp.float32),
            pltpu.VMEM((cells, 55, rows, 128), jnp.float32),
            pltpu.SemaphoreType.DMA((3, cells // 8)),
            pltpu.SemaphoreType.DMA((cells // 8,)),
        ],
        compiler_params=pltpu.CompilerParams(vmem_limit_bytes=60 * 1024 * 1024),
    )(vis_s, jac_s, src_s)

    ends = jnp.stack([factors[0], factors[cells - 1]]).reshape(2 * 55, parts, chunk)
    sent = jnp.transpose(ends, (1, 0, 2))
    gathered = lax.all_to_all(sent, "line", 0, 0, tiled=True)
    answers = pl.pallas_call(
        reduced_kernel,
        out_shape=whole((parts, 10, chunk)),
        in_specs=[vmem],
        out_specs=vmem,
        scratch_shapes=[pltpu.VMEM((parts + 1, 60, chunk), jnp.float32)],
    )(gathered)
    back = lax.all_to_all(answers, "line", 0, 0, tiled=True)
    bounds = jnp.moveaxis(back, 1, 0).reshape(10, rows, 128)
    blocks = cells // 8
    delta_s = pl.pallas_call(
        combine_kernel,
        out_shape=whole((NV, blocks, rows * 8, 128)),
        grid=(blocks,),
        in_specs=[
            pl.BlockSpec((8, 55, rows, 128), lambda c: (c, 0, 0, 0)),
            pl.BlockSpec((10, rows, 128), lambda c: (0, 0, 0)),
        ],
        out_specs=pl.BlockSpec((NV, 1, rows * 8, 128), lambda c: (0, c, 0, 0)),
    )(factors, bounds)
    delta = jnp.swapaxes(delta_s.reshape(NV, blocks, rows, 8, 128), 2, 3).reshape(NV, cells, line_count)
    return jnp.transpose(delta, (1, 0, 2))


def solution(mesh):
    placed = (
        P("line", None, "plane"),
        P("line", None, "plane"),
        P("line", "plane"),
        P("line", None, None, "plane"),
    )
    return jax.shard_map(
        per_device, mesh=mesh, in_specs=placed, out_specs=P("line", None, "plane"), check_vma=False
    )
```

```python
import jax
import jax.numpy as jnp
from jax import lax
from jax.experimental import pallas as pl
from jax.experimental.pallas import tpu as pltpu
from jax.sharding import PartitionSpec as P

courant = 10.0
NV = 5


def padded(block, sides, width):
    for axis, dim in sides:
        count = lax.axis_size(axis)
        forward = [(i, i + 1) for i in range(count - 1)]
        backward = [(target, source) for source, target in forward]
        low = lax.ppermute(
            lax.slice_in_dim(block, block.shape[dim] - width, None, axis=dim), axis, forward
        )
        high = lax.ppermute(lax.slice_in_dim(block, 0, width, axis=dim), axis, backward)
        block = jnp.concatenate([low, block, high], axis=dim)
    return block


def matmul(a, b, rows, inner, cols):
    out = []
    for r in range(rows):
        line = []
        for c in range(cols):
            acc = a[r][0] * b[0][c]
            for k in range(1, inner):
                acc = acc + a[r][k] * b[k][c]
            line.append(acc)
        out.append(line)
    return out


def gauss_jordan(matrix, columns):
    matrix = [row[:] for row in matrix]
    columns = [row[:] for row in columns]
    for k in range(NV):
        inverse = 1.0 / matrix[k][k]
        pivot = [matrix[k][j] * inverse for j in range(k + 1, NV)]
        chosen = [x * inverse for x in columns[k]]
        for r in range(NV):
            if r == k:
                continue
            factor = matrix[r][k]
            for jj, j in enumerate(range(k + 1, NV)):
                matrix[r][j] = matrix[r][j] - factor * pivot[jj]
            columns[r] = [x - factor * y for x, y in zip(columns[r], chosen)]
        matrix[k] = [None] * (k + 1) + pivot
        columns[k] = chosen
    return columns


def grid_of(flat, rows, cols):
    return [[flat[r * cols + c] for c in range(cols)] for r in range(rows)]


def flat_of(grid):
    return [x for row in grid for x in row]


def factor_kernel(vis_hbm, jac_hbm, src_hbm, out_hbm, vis_ref, jac_ref, src_ref, out_ref, in_sem, out_sem):
    cells = out_ref.shape[0]
    blocks = cells // 8
    tile = out_ref.shape[2:]
    rows = tile[0]
    zero = jnp.zeros(tile, jnp.float32)
    one = jnp.ones(tile, jnp.float32)

    def arrivals(b):
        return [
            pltpu.make_async_copy(vis_hbm.at[b], vis_ref.at[b], in_sem.at[0, b]),
            pltpu.make_async_copy(jac_hbm.at[:, b], jac_ref.at[:, b], in_sem.at[1, b]),
            pltpu.make_async_copy(src_hbm.at[:, b], src_ref.at[:, b], in_sem.at[2, b]),
        ]

    def departure(b):
        return pltpu.make_async_copy(out_ref.at[pl.ds(b * 8, 8)], out_hbm.at[pl.ds(b * 8, 8)], out_sem.at[b])

    for b in range(blocks):
        for copy in arrivals(b):
            copy.start()

    def forward(i, carry):
        @pl.when(i % 8 == 0)
        def _():
            for copy in arrivals(i // 8):
                copy.wait()

        c_prev = grid_of(carry[0:25], NV, NV)
        g_prev = [[x] for x in carry[25:30]]
        w_prev = grid_of(carry[30:55], NV, NV)
        block = i // 8
        picked = pl.ds(i % 8, rows, stride=8)
        spread = vis_ref[block, picked, :]
        jac = [[jac_ref[a * NV + b, block, picked, :] for b in range(NV)] for a in range(NV)]
        lower = [[(-spread - jac[a][b]) if a == b else (-jac[a][b]) for b in range(NV)] for a in range(NV)]
        upper = [[(-spread + jac[a][b]) if a == b else jac[a][b] for b in range(NV)] for a in range(NV)]
        centre = 1.0 + 2.0 * spread
        lc = matmul(lower, c_prev, NV, NV, NV)
        schur = [[(centre - lc[a][c]) if a == c else (-lc[a][c]) for c in range(NV)] for a in range(NV)]
        lg = matmul(lower, g_prev, NV, NV, 1)
        lw = matmul(lower, w_prev, NV, NV, NV)
        cols = []
        for a in range(NV):
            cols.append(upper[a] + [src_ref[a, block, picked, :] - lg[a][0]] + [-x for x in lw[a]])
        sol = gauss_jordan(schur, cols)
        c_new = [row[0:NV] for row in sol]
        g_new = [row[NV] for row in sol]
        w_new = [row[NV + 1:] for row in sol]
        flat = flat_of(c_new) + g_new + flat_of(w_new)
        for k in range(55):
            out_ref[i, k] = flat[k]
        return tuple(flat)

    init = [zero] * 30 + flat_of([[(-one if a == b else zero) for b in range(NV)] for a in range(NV)])
    lax.fori_loop(0, cells, forward, tuple(init))

    def backward(step, carry):
        i = cells - 1 - step
        nxt = [[carry[a]] + list(carry[5 + a * 5:10 + a * 5]) + list(carry[30 + a * 5:35 + a * 5]) for a in range(NV)]
        c_i = [[out_ref[i, a * NV + b] for b in range(NV)] for a in range(NV)]
        g_i = [out_ref[i, 25 + a] for a in range(NV)]
        w_i = [[out_ref[i, 30 + a * NV + b] for b in range(NV)] for a in range(NV)]
        prod = matmul(c_i, nxt, NV, NV, 11)
        y = [g_i[a] - prod[a][0] for a in range(NV)]
        w = [[w_i[a][b] - prod[a][1 + b] for b in range(NV)] for a in range(NV)]
        v = [[-prod[a][6 + b] for b in range(NV)] for a in range(NV)]
        flat = y + flat_of(w) + flat_of(v)
        for k in range(55):
            out_ref[i, k] = flat[k]

        @pl.when(i % 8 == 0)
        def _():
            departure(i // 8).start()

        return tuple(flat)

    init = [zero] * 30 + flat_of([[(-one if a == b else zero) for b in range(NV)] for a in range(NV)])
    lax.fori_loop(0, cells, backward, tuple(init))
    for b in range(blocks):
        departure(b).wait()


def interface_step(tail, head, carry):
    x_prev = grid_of(carry[0:25], NV, NV)
    u_prev = [[x] for x in carry[25:30]]
    y63 = tail[0:5]
    w63 = grid_of(tail[5:30], NV, NV)
    v63 = grid_of(tail[30:55], NV, NV)
    y0 = head[0:5]
    w0 = grid_of(head[5:30], NV, NV)
    v0 = grid_of(head[30:55], NV, NV)
    wx = matmul(w63, x_prev, NV, NV, NV)
    m = [[v63[a][b] - wx[a][b] for b in range(NV)] for a in range(NV)]
    wu = matmul(w63, u_prev, NV, NV, 1)
    av = [[y63[a] - wu[a][0]] for a in range(NV)]
    wm = matmul(w0, m, NV, NV, NV)
    k_mat = [[(1.0 - wm[a][b]) if a == b else (-wm[a][b]) for b in range(NV)] for a in range(NV)]
    wa = matmul(w0, av, NV, NV, 1)
    cols = [v0[a] + [y0[a] - wa[a][0]] for a in range(NV)]
    sol = gauss_jordan(k_mat, cols)
    y_new = [r[0:NV] for r in sol]
    v_new = [[r[NV]] for r in sol]
    my = matmul(m, y_new, NV, NV, NV)
    x_new = [[-my[a][b] for b in range(NV)] for a in range(NV)]
    mv = matmul(m, v_new, NV, NV, 1)
    u_new = [av[a][0] - mv[a][0] for a in range(NV)]
    flat = flat_of(x_new) + flat_of(y_new) + u_new + [r[0] for r in v_new]
    return flat, tuple(flat[0:25] + u_new)


def reduced_kernel(ends_ref, out_ref, keep_ref):
    parts = ends_ref.shape[0]
    lanes = ends_ref.shape[2]
    zero = jnp.zeros((1, lanes), jnp.float32)

    def rows_of(p, first):
        if first == 0:
            return [ends_ref[p, k:k + 1, :] for k in range(55)]
        return [pltpu.roll(ends_ref[p, k:k + 1, :], lanes // 2, 1) for k in range(55)]

    def keep(q, flat):
        for k in range(60):
            keep_ref[q, k:k + 1, :] = flat[k]

    flat, carry = interface_step([zero] * 55, rows_of(0, 0), tuple([zero] * 30))
    keep(0, flat)

    def forward(q, carry):
        flat, carry = interface_step(rows_of(q - 1, 55), rows_of(q, 0), carry)
        keep(q, flat)
        return carry

    carry = lax.fori_loop(1, parts, forward, carry)
    flat, carry = interface_step(rows_of(parts - 1, 55), [zero] * 55, carry)
    keep(parts, flat)

    h_next = [[zero] for _ in range(NV)]
    for q in range(parts, -1, -1):
        x_q = [[keep_ref[q, a * NV + b:a * NV + b + 1, :] for b in range(NV)] for a in range(NV)]
        y_q = [[keep_ref[q, 25 + a * NV + b:26 + a * NV + b, :] for b in range(NV)] for a in range(NV)]
        u_q = [keep_ref[q, 50 + a:51 + a, :] for a in range(NV)]
        v_q = [keep_ref[q, 55 + a:56 + a, :] for a in range(NV)]
        xh = matmul(x_q, h_next, NV, NV, 1)
        yh = matmul(y_q, h_next, NV, NV, 1)
        t_prev = [u_q[a] - xh[a][0] for a in range(NV)]
        h_here = [v_q[a] - yh[a][0] for a in range(NV)]
        if q <= parts - 1:
            for a in range(NV):
                out_ref[q, a:a + 1, :] = t_prev[a]
        if q >= 1:
            for a in range(NV):
                out_ref[q - 1, 5 + a:6 + a, :] = h_here[a]
        h_next = [[x] for x in h_here]


def combine_kernel(fac_ref, bnd_ref, out_ref):
    rows = fac_ref.shape[2]
    before = [bnd_ref[b] for b in range(NV)]
    after = [bnd_ref[NV + b] for b in range(NV)]
    for c in range(fac_ref.shape[0]):
        for a in range(NV):
            w_t = fac_ref[c, 5 + a * NV] * before[0]
            v_h = fac_ref[c, 30 + a * NV] * after[0]
            for b in range(1, NV):
                w_t = w_t + fac_ref[c, 5 + a * NV + b] * before[b]
                v_h = v_h + fac_ref[c, 30 + a * NV + b] * after[b]
            out_ref[a, 0, pl.ds(c, rows, stride=8), :] = fac_ref[c, a] - w_t - v_h


def whole(shape):
    return jax.ShapeDtypeStruct(shape, jnp.float32)


def stored_order(array, lead):
    *head, cells, lines = array.shape
    rows = lines // 128
    split = array.reshape(*head, cells // 8, 8, rows, 128)
    return jnp.swapaxes(split, -3, -2).reshape(*head, cells // 8, rows * 8, 128)


def per_device(flux_x, flux_z, viscous, jacobian):
    cells, line_count = viscous.shape
    rows = line_count // 128
    parts = lax.axis_size("line")
    chunk = line_count // parts
    stream = padded(flux_x, (("line", 0),), 1)
    across = padded(flux_z, (("plane", 2),), 1)
    source = -0.5 * courant * (stream[2:] - stream[:-2]) - 0.5 * courant * (
        across[:, :, 2:] - across[:, :, :-2]
    )
    src_s = stored_order(jnp.transpose(source, (1, 0, 2)), 1)
    jac_s = stored_order(jnp.transpose(jacobian, (1, 2, 0, 3)).reshape(NV * NV, cells, line_count), 1)
    vis_s = stored_order(viscous, 0)
    vmem = pl.BlockSpec(memory_space=pltpu.VMEM)
    hbm = pl.BlockSpec(memory_space=pl.ANY)
    factors = pl.pallas_call(
        factor_kernel,
        out_shape=whole((cells, 55, rows, 128)),
        in_specs=[hbm, hbm, hbm],
        out_specs=hbm,
        scratch_shapes=[
            pltpu.VMEM(vis_s.shape, jnp.float32),
            pltpu.VMEM(jac_s.shape, jnp.float32),
            pltpu.VMEM(src_s.shape, jnp.float32),
            pltpu.VMEM((cells, 55, rows, 128), jnp.float32),
            pltpu.SemaphoreType.DMA((3, cells // 8)),
            pltpu.SemaphoreType.DMA((cells // 8,)),
        ],
        compiler_params=pltpu.CompilerParams(vmem_limit_bytes=60 * 1024 * 1024),
    )(vis_s, jac_s, src_s)

    ends = jnp.stack([factors[0], factors[cells - 1]]).reshape(2, 55, parts, chunk)
    sent = jnp.transpose(ends, (2, 1, 0, 3)).reshape(parts, 55, 2 * chunk)
    gathered = lax.all_to_all(sent, "line", 0, 0, tiled=True)
    answers = pl.pallas_call(
        reduced_kernel,
        out_shape=whole((parts, 10, 2 * chunk)),
        in_specs=[vmem],
        out_specs=vmem,
        scratch_shapes=[pltpu.VMEM((parts + 1, 60, 2 * chunk), jnp.float32)],
    )(gathered)
    back = lax.all_to_all(answers[:, :, :chunk], "line", 0, 0, tiled=True)
    bounds = jnp.moveaxis(back, 1, 0).reshape(10, rows, 128)
    blocks = cells // 8
    delta_s = pl.pallas_call(
        combine_kernel,
        out_shape=whole((NV, blocks, rows * 8, 128)),
        grid=(blocks,),
        in_specs=[
            pl.BlockSpec((8, 55, rows, 128), lambda c: (c, 0, 0, 0)),
            pl.BlockSpec((10, rows, 128), lambda c: (0, 0, 0)),
        ],
        out_specs=pl.BlockSpec((NV, 1, rows * 8, 128), lambda c: (0, c, 0, 0)),
    )(factors, bounds)
    delta = jnp.swapaxes(delta_s.reshape(NV, blocks, rows, 8, 128), 2, 3).reshape(NV, cells, line_count)
    return jnp.transpose(delta, (1, 0, 2))


def solution(mesh):
    placed = (
        P("line", None, "plane"),
        P("line", None, "plane"),
        P("line", "plane"),
        P("line", None, None, "plane"),
    )
    return jax.shard_map(
        per_device, mesh=mesh, in_specs=placed, out_specs=P("line", None, "plane"), check_vma=False
    )
```

```python
import jax
import jax.numpy as jnp
from jax import lax
from jax.experimental import pallas as pl
from jax.experimental.pallas import tpu as pltpu
from jax.sharding import PartitionSpec as P

courant = 10.0
NV = 5


def padded(block, sides, width):
    for axis, dim in sides:
        count = lax.axis_size(axis)
        forward = [(i, i + 1) for i in range(count - 1)]
        backward = [(target, source) for source, target in forward]
        low = lax.ppermute(
            lax.slice_in_dim(block, block.shape[dim] - width, None, axis=dim), axis, forward
        )
        high = lax.ppermute(lax.slice_in_dim(block, 0, width, axis=dim), axis, backward)
        block = jnp.concatenate([low, block, high], axis=dim)
    return block


def matmul(a, b, rows, inner, cols):
    out = []
    for r in range(rows):
        line = []
        for c in range(cols):
            acc = a[r][0] * b[0][c]
            for k in range(1, inner):
                acc = acc + a[r][k] * b[k][c]
            line.append(acc)
        out.append(line)
    return out


def gauss_jordan(matrix, columns):
    matrix = [row[:] for row in matrix]
    columns = [row[:] for row in columns]
    for k in range(NV):
        inverse = 1.0 / matrix[k][k]
        pivot = [matrix[k][j] * inverse for j in range(k + 1, NV)]
        chosen = [x * inverse for x in columns[k]]
        for r in range(NV):
            if r == k:
                continue
            factor = matrix[r][k]
            for jj, j in enumerate(range(k + 1, NV)):
                matrix[r][j] = matrix[r][j] - factor * pivot[jj]
            columns[r] = [x - factor * y for x, y in zip(columns[r], chosen)]
        matrix[k] = [None] * (k + 1) + pivot
        columns[k] = chosen
    return columns


def grid_of(flat, rows, cols):
    return [[flat[r * cols + c] for c in range(cols)] for r in range(rows)]


def flat_of(grid):
    return [x for row in grid for x in row]


def factor_kernel(
    edge_x, edge_lo, edge_hi, vis_hbm, jac_hbm, fx_hbm, fz_hbm, out_hbm,
    vis_ref, jac_ref, fx_ref, fz_ref, out_ref, in_sem, out_sem,
):
    cells = out_ref.shape[0]
    blocks = cells // 8
    tile = out_ref.shape[2:]
    rows = tile[0]
    zero = jnp.zeros(tile, jnp.float32)
    one = jnp.ones(tile, jnp.float32)

    def arrivals(b):
        return [
            pltpu.make_async_copy(vis_hbm.at[b], vis_ref.at[b], in_sem.at[0, b]),
            pltpu.make_async_copy(jac_hbm.at[:, b], jac_ref.at[:, b], in_sem.at[1, b]),
            pltpu.make_async_copy(fx_hbm.at[:, b], fx_ref.at[:, b], in_sem.at[2, b]),
            pltpu.make_async_copy(fz_hbm.at[:, b], fz_ref.at[:, b], in_sem.at[3, b]),
        ]

    lane = lax.broadcasted_iota(jnp.int32, tile, 1)
    row = lax.broadcasted_iota(jnp.int32, tile, 0)
    lane_up = pltpu.roll(lane, 127, 1) == (lane + 1) % 128
    row_up = pltpu.roll(row, rows - 1, 0) == (row + 1) % rows

    def following(x):
        ahead = jnp.where(lane_up, pltpu.roll(x, 127, 1), pltpu.roll(x, 1, 1))
        wrapped = jnp.where(row_up, pltpu.roll(ahead, rows - 1, 0), pltpu.roll(ahead, 1, 0))
        return jnp.where(lane == 127, wrapped, ahead)

    def preceding(x):
        behind = jnp.where(lane_up, pltpu.roll(x, 1, 1), pltpu.roll(x, 127, 1))
        wrapped = jnp.where(row_up, pltpu.roll(behind, 1, 0), pltpu.roll(behind, rows - 1, 0))
        return jnp.where(lane == 0, wrapped, behind)

    last_line = (lane == 127) & (row == rows - 1)
    first_line = (lane == 0) & (row == 0)

    def source_of(i, block, picked, a):
        low = jnp.maximum(i - 1, 0)
        high = jnp.minimum(i + 1, cells - 1)
        below = fx_ref[a, low // 8, pl.ds(low % 8, rows, stride=8), :]
        above = fx_ref[a, high // 8, pl.ds(high % 8, rows, stride=8), :]
        is_first = (i == 0).astype(jnp.float32)
        is_last = (i == cells - 1).astype(jnp.float32)
        below = (1.0 - is_first) * below + is_first * edge_x[0, a]
        above = (1.0 - is_last) * above + is_last * edge_x[1, a]
        across = fz_ref[a, block, picked, :]
        nxt = jnp.where(last_line, edge_hi[a, i], following(across))
        prv = jnp.where(first_line, edge_lo[a, i], preceding(across))
        return -0.5 * courant * (above - below) - 0.5 * courant * (nxt - prv)

    def departure(b):
        return pltpu.make_async_copy(out_ref.at[pl.ds(b * 8, 8)], out_hbm.at[pl.ds(b * 8, 8)], out_sem.at[b])

    for b in range(blocks):
        for copy in arrivals(b):
            copy.start()
    for copy in arrivals(0):
        copy.wait()

    def forward(i, carry):
        @pl.when((i % 8 == 0) & (i + 8 < cells))
        def _():
            for copy in arrivals(i // 8 + 1):
                copy.wait()

        c_prev = grid_of(carry[0:25], NV, NV)
        g_prev = [[x] for x in carry[25:30]]
        w_prev = grid_of(carry[30:55], NV, NV)
        block = i // 8
        picked = pl.ds(i % 8, rows, stride=8)
        spread = vis_ref[block, picked, :]
        jac = [[jac_ref[a * NV + b, block, picked, :] for b in range(NV)] for a in range(NV)]
        lower = [[(-spread - jac[a][b]) if a == b else (-jac[a][b]) for b in range(NV)] for a in range(NV)]
        upper = [[(-spread + jac[a][b]) if a == b else jac[a][b] for b in range(NV)] for a in range(NV)]
        centre = 1.0 + 2.0 * spread
        lc = matmul(lower, c_prev, NV, NV, NV)
        schur = [[(centre - lc[a][c]) if a == c else (-lc[a][c]) for c in range(NV)] for a in range(NV)]
        lg = matmul(lower, g_prev, NV, NV, 1)
        lw = matmul(lower, w_prev, NV, NV, NV)
        cols = []
        for a in range(NV):
            cols.append(upper[a] + [source_of(i, block, picked, a) - lg[a][0]] + [-x for x in lw[a]])
        sol = gauss_jordan(schur, cols)
        c_new = [row[0:NV] for row in sol]
        g_new = [row[NV] for row in sol]
        w_new = [row[NV + 1:] for row in sol]
        flat = flat_of(c_new) + g_new + flat_of(w_new)
        for k in range(55):
            out_ref[i, k] = flat[k]
        return tuple(flat)

    init = [zero] * 30 + flat_of([[(-one if a == b else zero) for b in range(NV)] for a in range(NV)])
    lax.fori_loop(0, cells, forward, tuple(init))

    def backward(step, carry):
        i = cells - 1 - step
        nxt = [[carry[a]] + list(carry[5 + a * 5:10 + a * 5]) + list(carry[30 + a * 5:35 + a * 5]) for a in range(NV)]
        c_i = [[out_ref[i, a * NV + b] for b in range(NV)] for a in range(NV)]
        g_i = [out_ref[i, 25 + a] for a in range(NV)]
        w_i = [[out_ref[i, 30 + a * NV + b] for b in range(NV)] for a in range(NV)]
        prod = matmul(c_i, nxt, NV, NV, 11)
        y = [g_i[a] - prod[a][0] for a in range(NV)]
        w = [[w_i[a][b] - prod[a][1 + b] for b in range(NV)] for a in range(NV)]
        v = [[-prod[a][6 + b] for b in range(NV)] for a in range(NV)]
        flat = y + flat_of(w) + flat_of(v)
        for k in range(55):
            out_ref[i, k] = flat[k]

        @pl.when(i % 8 == 0)
        def _():
            departure(i // 8).start()

        return tuple(flat)

    init = [zero] * 30 + flat_of([[(-one if a == b else zero) for b in range(NV)] for a in range(NV)])
    lax.fori_loop(0, cells, backward, tuple(init))
    for b in range(blocks):
        departure(b).wait()


def interface_step(tail, head, carry):
    x_prev = grid_of(carry[0:25], NV, NV)
    u_prev = [[x] for x in carry[25:30]]
    y63 = tail[0:5]
    w63 = grid_of(tail[5:30], NV, NV)
    v63 = grid_of(tail[30:55], NV, NV)
    y0 = head[0:5]
    w0 = grid_of(head[5:30], NV, NV)
    v0 = grid_of(head[30:55], NV, NV)
    wx = matmul(w63, x_prev, NV, NV, NV)
    m = [[v63[a][b] - wx[a][b] for b in range(NV)] for a in range(NV)]
    wu = matmul(w63, u_prev, NV, NV, 1)
    av = [[y63[a] - wu[a][0]] for a in range(NV)]
    wm = matmul(w0, m, NV, NV, NV)
    k_mat = [[(1.0 - wm[a][b]) if a == b else (-wm[a][b]) for b in range(NV)] for a in range(NV)]
    wa = matmul(w0, av, NV, NV, 1)
    cols = [v0[a] + [y0[a] - wa[a][0]] for a in range(NV)]
    sol = gauss_jordan(k_mat, cols)
    y_new = [r[0:NV] for r in sol]
    v_new = [[r[NV]] for r in sol]
    my = matmul(m, y_new, NV, NV, NV)
    x_new = [[-my[a][b] for b in range(NV)] for a in range(NV)]
    mv = matmul(m, v_new, NV, NV, 1)
    u_new = [av[a][0] - mv[a][0] for a in range(NV)]
    flat = flat_of(x_new) + flat_of(y_new) + u_new + [r[0] for r in v_new]
    return flat, tuple(flat[0:25] + u_new)


def reduced_kernel(ends_ref, out_ref, keep_ref):
    parts = ends_ref.shape[0]
    lanes = ends_ref.shape[2]
    zero = jnp.zeros((1, lanes), jnp.float32)

    def rows_of(p, first):
        return [ends_ref[p, first + k:first + k + 1, :] for k in range(55)]

    def keep(q, flat):
        for k in range(60):
            keep_ref[q, k:k + 1, :] = flat[k]

    flat, carry = interface_step([zero] * 55, rows_of(0, 0), tuple([zero] * 30))
    keep(0, flat)

    def forward(q, carry):
        flat, carry = interface_step(rows_of(q - 1, 55), rows_of(q, 0), carry)
        keep(q, flat)
        return carry

    carry = lax.fori_loop(1, parts, forward, carry)
    flat, carry = interface_step(rows_of(parts - 1, 55), [zero] * 55, carry)
    keep(parts, flat)

    h_next = [[zero] for _ in range(NV)]
    for q in range(parts, -1, -1):
        x_q = [[keep_ref[q, a * NV + b:a * NV + b + 1, :] for b in range(NV)] for a in range(NV)]
        y_q = [[keep_ref[q, 25 + a * NV + b:26 + a * NV + b, :] for b in range(NV)] for a in range(NV)]
        u_q = [keep_ref[q, 50 + a:51 + a, :] for a in range(NV)]
        v_q = [keep_ref[q, 55 + a:56 + a, :] for a in range(NV)]
        xh = matmul(x_q, h_next, NV, NV, 1)
        yh = matmul(y_q, h_next, NV, NV, 1)
        t_prev = [u_q[a] - xh[a][0] for a in range(NV)]
        h_here = [v_q[a] - yh[a][0] for a in range(NV)]
        if q <= parts - 1:
            for a in range(NV):
                out_ref[q, a:a + 1, :] = t_prev[a]
        if q >= 1:
            for a in range(NV):
                out_ref[q - 1, 5 + a:6 + a, :] = h_here[a]
        h_next = [[x] for x in h_here]


def combine_kernel(fac_ref, bnd_ref, out_ref):
    rows = fac_ref.shape[2]
    before = [bnd_ref[b] for b in range(NV)]
    after = [bnd_ref[NV + b] for b in range(NV)]
    for c in range(fac_ref.shape[0]):
        for a in range(NV):
            w_t = fac_ref[c, 5 + a * NV] * before[0]
            v_h = fac_ref[c, 30 + a * NV] * after[0]
            for b in range(1, NV):
                w_t = w_t + fac_ref[c, 5 + a * NV + b] * before[b]
                v_h = v_h + fac_ref[c, 30 + a * NV + b] * after[b]
            out_ref[a, 0, pl.ds(c, rows, stride=8), :] = fac_ref[c, a] - w_t - v_h


def whole(shape):
    return jax.ShapeDtypeStruct(shape, jnp.float32)


def stored_order(array, lead):
    *head, cells, lines = array.shape
    rows = lines // 128
    split = array.reshape(*head, cells // 8, 8, rows, 128)
    return jnp.swapaxes(split, -3, -2).reshape(*head, cells // 8, rows * 8, 128)


def per_device(flux_x, flux_z, viscous, jacobian):
    cells, line_count = viscous.shape
    rows = line_count // 128
    parts = lax.axis_size("line")
    chunk = line_count // parts
    stream = padded(flux_x, (("line", 0),), 1)
    across = padded(flux_z, (("plane", 2),), 1)
    edge_x = jnp.stack([stream[0], stream[cells + 1]]).reshape(2, NV, rows, 128)
    edge_lo = jnp.transpose(across[:, :, 0])
    edge_hi = jnp.transpose(across[:, :, line_count + 1])
    fx_s = stored_order(jnp.transpose(flux_x, (1, 0, 2)), 1)
    fz_s = stored_order(jnp.transpose(flux_z, (1, 0, 2)), 1)
    jac_s = stored_order(jnp.transpose(jacobian, (1, 2, 0, 3)).reshape(NV * NV, cells, line_count), 1)
    vis_s = stored_order(viscous, 0)
    vmem = pl.BlockSpec(memory_space=pltpu.VMEM)
    hbm = pl.BlockSpec(memory_space=pl.ANY)
    smem = pl.BlockSpec(memory_space=pltpu.SMEM)
    factors = pl.pallas_call(
        factor_kernel,
        out_shape=whole((cells, 55, rows, 128)),
        in_specs=[vmem, smem, smem, hbm, hbm, hbm, hbm],
        out_specs=hbm,
        scratch_shapes=[
            pltpu.VMEM(vis_s.shape, jnp.float32),
            pltpu.VMEM(jac_s.shape, jnp.float32),
            pltpu.VMEM(fx_s.shape, jnp.float32),
            pltpu.VMEM(fz_s.shape, jnp.float32),
            pltpu.VMEM((cells, 55, rows, 128), jnp.float32),
            pltpu.SemaphoreType.DMA((4, cells // 8)),
            pltpu.SemaphoreType.DMA((cells // 8,)),
        ],
        compiler_params=pltpu.CompilerParams(vmem_limit_bytes=60 * 1024 * 1024),
    )(edge_x, edge_lo, edge_hi, vis_s, jac_s, fx_s, fz_s)

    ends = jnp.stack([factors[0], factors[cells - 1]]).reshape(2 * 55, parts, chunk)
    sent = jnp.transpose(ends, (1, 0, 2))
    gathered = lax.all_to_all(sent, "line", 0, 0, tiled=True)
    answers = pl.pallas_call(
        reduced_kernel,
        out_shape=whole((parts, 10, chunk)),
        in_specs=[vmem],
        out_specs=vmem,
        scratch_shapes=[pltpu.VMEM((parts + 1, 60, chunk), jnp.float32)],
    )(gathered)
    back = lax.all_to_all(answers, "line", 0, 0, tiled=True)
    bounds = jnp.moveaxis(back, 1, 0).reshape(10, rows, 128)
    blocks = cells // 8
    delta_s = pl.pallas_call(
        combine_kernel,
        out_shape=whole((NV, blocks, rows * 8, 128)),
        grid=(blocks,),
        in_specs=[
            pl.BlockSpec((8, 55, rows, 128), lambda c: (c, 0, 0, 0)),
            pl.BlockSpec((10, rows, 128), lambda c: (0, 0, 0)),
        ],
        out_specs=pl.BlockSpec((NV, 1, rows * 8, 128), lambda c: (0, c, 0, 0)),
    )(factors, bounds)
    delta = jnp.swapaxes(delta_s.reshape(NV, blocks, rows, 8, 128), 2, 3).reshape(NV, cells, line_count)
    return jnp.transpose(delta, (1, 0, 2))


def solution(mesh):
    placed = (
        P("line", None, "plane"),
        P("line", None, "plane"),
        P("line", "plane"),
        P("line", None, None, "plane"),
    )
    return jax.shard_map(
        per_device, mesh=mesh, in_specs=placed, out_specs=P("line", None, "plane"), check_vma=False
    )
```

```python
import jax
import jax.numpy as jnp
from jax import lax
from jax.experimental import pallas as pl
from jax.experimental.pallas import tpu as pltpu
from jax.sharding import PartitionSpec as P

courant = 10.0
NV = 5


def padded(block, sides, width):
    for axis, dim in sides:
        count = lax.axis_size(axis)
        forward = [(i, i + 1) for i in range(count - 1)]
        backward = [(target, source) for source, target in forward]
        low = lax.ppermute(
            lax.slice_in_dim(block, block.shape[dim] - width, None, axis=dim), axis, forward
        )
        high = lax.ppermute(lax.slice_in_dim(block, 0, width, axis=dim), axis, backward)
        block = jnp.concatenate([low, block, high], axis=dim)
    return block


def matmul(a, b, rows, inner, cols):
    out = []
    for r in range(rows):
        line = []
        for c in range(cols):
            acc = a[r][0] * b[0][c]
            for k in range(1, inner):
                acc = acc + a[r][k] * b[k][c]
            line.append(acc)
        out.append(line)
    return out


def gauss_jordan(matrix, columns):
    matrix = [row[:] for row in matrix]
    columns = [row[:] for row in columns]
    for k in range(NV):
        inverse = 1.0 / matrix[k][k]
        pivot = [matrix[k][j] * inverse for j in range(k + 1, NV)]
        chosen = [x * inverse for x in columns[k]]
        for r in range(NV):
            if r == k:
                continue
            factor = matrix[r][k]
            for jj, j in enumerate(range(k + 1, NV)):
                matrix[r][j] = matrix[r][j] - factor * pivot[jj]
            columns[r] = [x - factor * y for x, y in zip(columns[r], chosen)]
        matrix[k] = [None] * (k + 1) + pivot
        columns[k] = chosen
    return columns


def grid_of(flat, rows, cols):
    return [[flat[r * cols + c] for c in range(cols)] for r in range(rows)]


def flat_of(grid):
    return [x for row in grid for x in row]


def factor_kernel(
    edge_x, edge_lo, edge_hi, vis_hbm, jac_hbm, fx_hbm, fz_hbm, out_hbm,
    vis_ref, jac_ref, fx_ref, fz_ref, out_ref, in_sem, out_sem,
):
    cells = out_ref.shape[0]
    blocks = cells // 8
    tile = out_ref.shape[2:]
    rows = tile[0]
    zero = jnp.zeros(tile, jnp.float32)
    one = jnp.ones(tile, jnp.float32)

    def arrivals(b):
        return [
            pltpu.make_async_copy(vis_hbm.at[b], vis_ref.at[b], in_sem.at[0, b]),
            pltpu.make_async_copy(jac_hbm.at[:, b], jac_ref.at[:, b], in_sem.at[1, b]),
            pltpu.make_async_copy(fx_hbm.at[:, b], fx_ref.at[:, b], in_sem.at[2, b]),
            pltpu.make_async_copy(fz_hbm.at[:, b], fz_ref.at[:, b], in_sem.at[3, b]),
        ]

    lane = lax.broadcasted_iota(jnp.int32, tile, 1)
    row = lax.broadcasted_iota(jnp.int32, tile, 0)
    lane_up = pltpu.roll(lane, 127, 1) == (lane + 1) % 128
    row_up = pltpu.roll(row, rows - 1, 0) == (row + 1) % rows

    def neighbours(x):
        left = pltpu.roll(x, 127, 1)
        right = pltpu.roll(x, 1, 1)
        ahead = jnp.where(lane_up, left, right)
        behind = jnp.where(lane_up, right, left)
        ahead_wrap = jnp.where(row_up, pltpu.roll(ahead, rows - 1, 0), pltpu.roll(ahead, 1, 0))
        behind_wrap = jnp.where(row_up, pltpu.roll(behind, 1, 0), pltpu.roll(behind, rows - 1, 0))
        return jnp.where(lane == 127, ahead_wrap, ahead), jnp.where(lane == 0, behind_wrap, behind)

    last_line = (lane == 127) & (row == rows - 1)
    first_line = (lane == 0) & (row == 0)

    def source_of(i, block, picked, a):
        low = jnp.maximum(i - 1, 0)
        high = jnp.minimum(i + 1, cells - 1)
        below = fx_ref[a, low // 8, pl.ds(low % 8, rows, stride=8), :]
        above = fx_ref[a, high // 8, pl.ds(high % 8, rows, stride=8), :]
        is_first = (i == 0).astype(jnp.float32)
        is_last = (i == cells - 1).astype(jnp.float32)
        below = (1.0 - is_first) * below + is_first * edge_x[0, a]
        above = (1.0 - is_last) * above + is_last * edge_x[1, a]
        across = fz_ref[a, block, picked, :]
        following, preceding = neighbours(across)
        nxt = jnp.where(last_line, edge_hi[a, i], following)
        prv = jnp.where(first_line, edge_lo[a, i], preceding)
        return -0.5 * courant * (above - below) - 0.5 * courant * (nxt - prv)

    def departure(b):
        return pltpu.make_async_copy(out_ref.at[pl.ds(b * 8, 8)], out_hbm.at[pl.ds(b * 8, 8)], out_sem.at[b])

    for b in range(blocks):
        for copy in arrivals(b):
            copy.start()
    for copy in arrivals(0):
        copy.wait()

    def forward(i, carry):
        @pl.when((i % 8 == 0) & (i + 8 < cells))
        def _():
            for copy in arrivals(i // 8 + 1):
                copy.wait()

        c_prev = grid_of(carry[0:25], NV, NV)
        g_prev = [[x] for x in carry[25:30]]
        w_prev = grid_of(carry[30:55], NV, NV)
        block = i // 8
        picked = pl.ds(i % 8, rows, stride=8)
        spread = vis_ref[block, picked, :]
        jac = [[jac_ref[a * NV + b, block, picked, :] for b in range(NV)] for a in range(NV)]
        lower = [[(-spread - jac[a][b]) if a == b else (-jac[a][b]) for b in range(NV)] for a in range(NV)]
        upper = [[(-spread + jac[a][b]) if a == b else jac[a][b] for b in range(NV)] for a in range(NV)]
        centre = 1.0 + 2.0 * spread
        lc = matmul(lower, c_prev, NV, NV, NV)
        schur = [[(centre - lc[a][c]) if a == c else (-lc[a][c]) for c in range(NV)] for a in range(NV)]
        lg = matmul(lower, g_prev, NV, NV, 1)
        lw = matmul(lower, w_prev, NV, NV, NV)
        cols = []
        for a in range(NV):
            cols.append(upper[a] + [source_of(i, block, picked, a) - lg[a][0]] + [-x for x in lw[a]])
        sol = gauss_jordan(schur, cols)
        c_new = [row[0:NV] for row in sol]
        g_new = [row[NV] for row in sol]
        w_new = [row[NV + 1:] for row in sol]
        flat = flat_of(c_new) + g_new + flat_of(w_new)
        for k in range(55):
            out_ref[i, k] = flat[k]
        return tuple(flat)

    init = [zero] * 30 + flat_of([[(-one if a == b else zero) for b in range(NV)] for a in range(NV)])
    lax.fori_loop(0, cells, forward, tuple(init))

    def backward(step, carry):
        i = cells - 1 - step
        nxt = [[carry[a]] + list(carry[5 + a * 5:10 + a * 5]) + list(carry[30 + a * 5:35 + a * 5]) for a in range(NV)]
        c_i = [[out_ref[i, a * NV + b] for b in range(NV)] for a in range(NV)]
        g_i = [out_ref[i, 25 + a] for a in range(NV)]
        w_i = [[out_ref[i, 30 + a * NV + b] for b in range(NV)] for a in range(NV)]
        prod = matmul(c_i, nxt, NV, NV, 11)
        y = [g_i[a] - prod[a][0] for a in range(NV)]
        w = [[w_i[a][b] - prod[a][1 + b] for b in range(NV)] for a in range(NV)]
        v = [[-prod[a][6 + b] for b in range(NV)] for a in range(NV)]
        flat = y + flat_of(w) + flat_of(v)
        for k in range(55):
            out_ref[i, k] = flat[k]

        @pl.when(i % 8 == 0)
        def _():
            departure(i // 8).start()

        return tuple(flat)

    init = [zero] * 30 + flat_of([[(-one if a == b else zero) for b in range(NV)] for a in range(NV)])
    lax.fori_loop(0, cells, backward, tuple(init))
    for b in range(blocks):
        departure(b).wait()


def interface_step(tail, head, carry):
    x_prev = grid_of(carry[0:25], NV, NV)
    u_prev = [[x] for x in carry[25:30]]
    y63 = tail[0:5]
    w63 = grid_of(tail[5:30], NV, NV)
    v63 = grid_of(tail[30:55], NV, NV)
    y0 = head[0:5]
    w0 = grid_of(head[5:30], NV, NV)
    v0 = grid_of(head[30:55], NV, NV)
    wx = matmul(w63, x_prev, NV, NV, NV)
    m = [[v63[a][b] - wx[a][b] for b in range(NV)] for a in range(NV)]
    wu = matmul(w63, u_prev, NV, NV, 1)
    av = [[y63[a] - wu[a][0]] for a in range(NV)]
    wm = matmul(w0, m, NV, NV, NV)
    k_mat = [[(1.0 - wm[a][b]) if a == b else (-wm[a][b]) for b in range(NV)] for a in range(NV)]
    wa = matmul(w0, av, NV, NV, 1)
    cols = [v0[a] + [y0[a] - wa[a][0]] for a in range(NV)]
    sol = gauss_jordan(k_mat, cols)
    y_new = [r[0:NV] for r in sol]
    v_new = [[r[NV]] for r in sol]
    my = matmul(m, y_new, NV, NV, NV)
    x_new = [[-my[a][b] for b in range(NV)] for a in range(NV)]
    mv = matmul(m, v_new, NV, NV, 1)
    u_new = [av[a][0] - mv[a][0] for a in range(NV)]
    flat = flat_of(x_new) + flat_of(y_new) + u_new + [r[0] for r in v_new]
    return flat, tuple(flat[0:25] + u_new)


def reduced_kernel(ends_ref, out_ref, keep_ref):
    parts = ends_ref.shape[0]
    lanes = ends_ref.shape[2]
    zero = jnp.zeros((1, lanes), jnp.float32)

    def rows_of(p, first):
        return [ends_ref[p, first + k:first + k + 1, :] for k in range(55)]

    def keep(q, flat):
        for k in range(60):
            keep_ref[q, k:k + 1, :] = flat[k]

    flat, carry = interface_step([zero] * 55, rows_of(0, 0), tuple([zero] * 30))
    keep(0, flat)

    def forward(q, carry):
        flat, carry = interface_step(rows_of(q - 1, 55), rows_of(q, 0), carry)
        keep(q, flat)
        return carry

    carry = lax.fori_loop(1, parts, forward, carry)
    flat, carry = interface_step(rows_of(parts - 1, 55), [zero] * 55, carry)
    keep(parts, flat)

    h_next = [[zero] for _ in range(NV)]
    for q in range(parts, -1, -1):
        x_q = [[keep_ref[q, a * NV + b:a * NV + b + 1, :] for b in range(NV)] for a in range(NV)]
        y_q = [[keep_ref[q, 25 + a * NV + b:26 + a * NV + b, :] for b in range(NV)] for a in range(NV)]
        u_q = [keep_ref[q, 50 + a:51 + a, :] for a in range(NV)]
        v_q = [keep_ref[q, 55 + a:56 + a, :] for a in range(NV)]
        xh = matmul(x_q, h_next, NV, NV, 1)
        yh = matmul(y_q, h_next, NV, NV, 1)
        t_prev = [u_q[a] - xh[a][0] for a in range(NV)]
        h_here = [v_q[a] - yh[a][0] for a in range(NV)]
        if q <= parts - 1:
            for a in range(NV):
                out_ref[q, a:a + 1, :] = t_prev[a]
        if q >= 1:
            for a in range(NV):
                out_ref[q - 1, 5 + a:6 + a, :] = h_here[a]
        h_next = [[x] for x in h_here]


def combine_kernel(fac_ref, bnd_ref, out_ref):
    rows = fac_ref.shape[2]
    before = [bnd_ref[b] for b in range(NV)]
    after = [bnd_ref[NV + b] for b in range(NV)]
    for c in range(fac_ref.shape[0]):
        for a in range(NV):
            w_t = fac_ref[c, 5 + a * NV] * before[0]
            v_h = fac_ref[c, 30 + a * NV] * after[0]
            for b in range(1, NV):
                w_t = w_t + fac_ref[c, 5 + a * NV + b] * before[b]
                v_h = v_h + fac_ref[c, 30 + a * NV + b] * after[b]
            out_ref[a, 0, pl.ds(c, rows, stride=8), :] = fac_ref[c, a] - w_t - v_h


def whole(shape):
    return jax.ShapeDtypeStruct(shape, jnp.float32)


def stored_order(array, lead):
    *head, cells, lines = array.shape
    rows = lines // 128
    split = array.reshape(*head, cells // 8, 8, rows, 128)
    return jnp.swapaxes(split, -3, -2).reshape(*head, cells // 8, rows * 8, 128)


def per_device(flux_x, flux_z, viscous, jacobian):
    cells, line_count = viscous.shape
    rows = line_count // 128
    parts = lax.axis_size("line")
    chunk = line_count // parts
    stream = padded(flux_x, (("line", 0),), 1)
    across = padded(flux_z, (("plane", 2),), 1)
    edge_x = jnp.stack([stream[0], stream[cells + 1]]).reshape(2, NV, rows, 128)
    edge_lo = jnp.transpose(across[:, :, 0])
    edge_hi = jnp.transpose(across[:, :, line_count + 1])
    fx_s = stored_order(jnp.transpose(flux_x, (1, 0, 2)), 1)
    fz_s = stored_order(jnp.transpose(flux_z, (1, 0, 2)), 1)
    jac_s = stored_order(jnp.transpose(jacobian, (1, 2, 0, 3)).reshape(NV * NV, cells, line_count), 1)
    vis_s = stored_order(viscous, 0)
    vmem = pl.BlockSpec(memory_space=pltpu.VMEM)
    hbm = pl.BlockSpec(memory_space=pl.ANY)
    smem = pl.BlockSpec(memory_space=pltpu.SMEM)
    factors = pl.pallas_call(
        factor_kernel,
        out_shape=whole((cells, 55, rows, 128)),
        in_specs=[vmem, smem, smem, hbm, hbm, hbm, hbm],
        out_specs=hbm,
        scratch_shapes=[
            pltpu.VMEM(vis_s.shape, jnp.float32),
            pltpu.VMEM(jac_s.shape, jnp.float32),
            pltpu.VMEM(fx_s.shape, jnp.float32),
            pltpu.VMEM(fz_s.shape, jnp.float32),
            pltpu.VMEM((cells, 55, rows, 128), jnp.float32),
            pltpu.SemaphoreType.DMA((4, cells // 8)),
            pltpu.SemaphoreType.DMA((cells // 8,)),
        ],
        compiler_params=pltpu.CompilerParams(vmem_limit_bytes=60 * 1024 * 1024),
    )(edge_x, edge_lo, edge_hi, vis_s, jac_s, fx_s, fz_s)

    ends = jnp.stack([factors[0], factors[cells - 1]]).reshape(2 * 55, parts, chunk)
    sent = jnp.transpose(ends, (1, 0, 2))
    gathered = lax.all_to_all(sent, "line", 0, 0, tiled=True)
    answers = pl.pallas_call(
        reduced_kernel,
        out_shape=whole((parts, 10, chunk)),
        in_specs=[vmem],
        out_specs=vmem,
        scratch_shapes=[pltpu.VMEM((parts + 1, 60, chunk), jnp.float32)],
    )(gathered)
    back = lax.all_to_all(answers, "line", 0, 0, tiled=True)
    bounds = jnp.moveaxis(back, 1, 0).reshape(10, rows, 128)
    blocks = cells // 8
    delta_s = pl.pallas_call(
        combine_kernel,
        out_shape=whole((NV, blocks, rows * 8, 128)),
        grid=(blocks,),
        in_specs=[
            pl.BlockSpec((8, 55, rows, 128), lambda c: (c, 0, 0, 0)),
            pl.BlockSpec((10, rows, 128), lambda c: (0, 0, 0)),
        ],
        out_specs=pl.BlockSpec((NV, 1, rows * 8, 128), lambda c: (0, c, 0, 0)),
    )(factors, bounds)
    delta = jnp.swapaxes(delta_s.reshape(NV, blocks, rows, 8, 128), 2, 3).reshape(NV, cells, line_count)
    return jnp.transpose(delta, (1, 0, 2))


def solution(mesh):
    placed = (
        P("line", None, "plane"),
        P("line", None, "plane"),
        P("line", "plane"),
        P("line", None, None, "plane"),
    )
    return jax.shard_map(
        per_device, mesh=mesh, in_specs=placed, out_specs=P("line", None, "plane"), check_vma=False
    )
```
